128 devices in a mesh: lat: 8 (over z, x_lo), lon: 16 (over y, x_hi, core).
Axes of the slice: x: 4 (x_hi: 2, x_lo: 2; x = x_hi * 2 + x_lo), y: 4, z: 4, core: 2. Of those that a mesh axis runs over, the one named last changes fastest.
Arguments:
- radiances: bfloat16 [131072, 8461], P(('lat', 'lon')), may hold values from -6 to 6
- project_weight: bfloat16 [8461, 256], replicated, may hold values from -0.0625 to 0.0625
- tile_ids: int32 [131072], P(('lat', 'lon')), may hold values from 0 to 127, as said below
- slot_offsets: int32 [131072], P(('lat', 'lon')), may hold values from 0 to 2559, as said below
- tile_counts: int32 [8, 16], P('lat', 'lon'), may hold values from 512 to 2560, as said below
- setconv_weights: bfloat16 [512, 512, 2560], P('lat', 'lon'), may hold values from 0.049804688 to 1
- conv1_weight: bfloat16 [3, 3, 256, 256], replicated, may hold values from -0.125 to 0.125
- conv2_weight: bfloat16 [3, 3, 256, 256], replicated, may hold values from -0.125 to 0.125
Outputs:
- encoded: bfloat16 [128, 128, 256], P('lat', 'lon')
The draws below stay inside these ranges and needn't reach their ends.
Inputs may be any that keep to these rules, and one draw needn't show every extreme that they name: `tile_ids`: A device's observations bound for one tile stand next to each other; one device sends at most 28 observations to one tile, a number reached in every draw. `slot_offsets`: the observations bound for one tile hold the offsets 0 to its count minus 1, each once. `tile_counts`: each entry is the number of observations whose tile_ids name that tile; 2560 is reached in every draw.
All inputs are finite; a program needn't handle non-finite values.
Results may differ from the reference program's by a relative error of at most 0.009.
Values may be sent and summed in bfloat16 or wider, within the bound.
No kernel may reach another device: no remote copies, remote signals or barrier semaphores. Data moves between devices by JAX's collectives and lax.ppermute only.
A program may use at most 512 MiB of HBM per device.

```python
import jax
import jax.numpy as jnp
import numpy as np
from jax import lax

CH_RAW = 8461
CHANNELS = 256
CLAT = 64
CLON = 32
OBS_DEV = 1024
SLOTS = 2560
OBSERVATIONS = 131072
NLAT = 512
NLON = 512
N_LAT = 8
N_LON = 16
DEVICES = 128


def observation_plan(key):
    unit_share = DEVICES // 16
    pair_mean = OBS_DEV // DEVICES
    level_table = np.concatenate([np.full(5 * unit_share, 0), np.full(3 * unit_share, 1), np.full(5 * unit_share, 3), np.full(2 * unit_share, 4), np.full(unit_share, 6)]).astype(np.int32)
    levels = jnp.asarray(level_table) * (pair_mean // 4)
    order = jax.random.permutation(jax.random.fold_in(key, 11), DEVICES)
    base_load = levels[order]
    hot_rank = jax.random.permutation(jax.random.fold_in(key, 12), DEVICES)
    hot_load = jnp.where(hot_rank < DEVICES // 4, 2 * pair_mean, 0).astype(jnp.int32)
    sources = jnp.arange(DEVICES, dtype=jnp.int32)[:, None]
    targets = jnp.arange(DEVICES, dtype=jnp.int32)[None, :]
    pair_load = base_load[(targets - sources) % DEVICES] + hot_load[None, :]
    tile_total = jnp.sum(pair_load, axis=0)
    pair_start = jnp.cumsum(pair_load, axis=0) - pair_load

    def one_loader(source):
        tile_order = (source + jnp.arange(DEVICES, dtype=jnp.int32)) % DEVICES
        run_length = pair_load[source, tile_order]
        run_begin = jnp.cumsum(run_length) - run_length
        run_index = jnp.repeat(jnp.arange(DEVICES, dtype=jnp.int32), run_length, total_repeat_length=OBS_DEV)
        loader_ids = tile_order[run_index]
        within_run = jnp.arange(OBS_DEV, dtype=jnp.int32) - run_begin[run_index]
        loader_offsets = pair_start[source, loader_ids] + within_run
        return (loader_ids, loader_offsets)
    all_ids, all_offsets = jax.vmap(one_loader)(jnp.arange(DEVICES, dtype=jnp.int32))
    return (all_ids.reshape(-1).astype(jnp.int32), all_offsets.reshape(-1).astype(jnp.int32), tile_total.astype(jnp.int32))


def draw_tile_ids(key, part):
    return observation_plan(key)[0]


def draw_slot_offsets(key, part):
    return observation_plan(key)[1]


def draw_tile_counts(key, part):
    return observation_plan(key)[2].reshape(-1, NLON // CLON)


def shard_levels(stream_key, extent, cuts, smallest, top_value):
    def one(axis_at, shards_of):
        steps = jax.random.uniform(jax.random.fold_in(jax.random.fold_in(stream_key, 6), axis_at), (shards_of,), jnp.float32, smallest / len(cuts), top_value / len(cuts))
        return jnp.repeat(jnp.exp(steps), extent[axis_at] // shards_of).reshape((-1,) + (1,) * (len(extent) - axis_at - 1))

    loudness = one(*cuts[0])
    for cut in cuts[1:]:
        loudness = loudness * one(*cut)
    return loudness


def normal_values(rng, shape, width, reach, split=(), held_as=jnp.bfloat16):
    drawn = width * jax.random.normal(rng, shape, jnp.float32)
    if split:
        drawn = drawn * shard_levels(rng, shape, split, -0.22, 0.18)
    return jnp.clip(drawn, -reach, reach).astype(held_as)


def setup_inputs(seed: int = 0) -> dict:
    key_list = jax.random.split(jax.random.key(seed), 9)
    return {
        "radiances": normal_values(key_list[0], (OBSERVATIONS, CH_RAW), 1.0, 6.0, ((0, 128),)),
        "project_weight": normal_values(key_list[1], (CH_RAW, CHANNELS), CH_RAW ** -0.5, 0.0625),
        "tile_ids": draw_tile_ids(jax.random.fold_in(key_list[8], 71), 0),
        "slot_offsets": draw_slot_offsets(jax.random.fold_in(key_list[8], 71), 0),
        "tile_counts": draw_tile_counts(jax.random.fold_in(key_list[8], 71), 0),
        "setconv_weights": jnp.clip(0.049804688 + 0.9501953 * jax.random.uniform(key_list[5], (NLAT, NLON, SLOTS), jnp.float32) ** shard_levels(key_list[5], (NLAT, NLON, SLOTS), ((0, 8), (1, 16)), -0.2, 0.2), 0.049804688, 1.0).astype(jnp.bfloat16),
        "conv1_weight": normal_values(key_list[6], (3, 3, CHANNELS, CHANNELS), (9 * CHANNELS) ** -0.5, 0.125),
        "conv2_weight": normal_values(key_list[7], (3, 3, CHANNELS, CHANNELS), (9 * CHANNELS) ** -0.5, 0.125),
    }


def project_rows(radiances, project_weight):
    blocks = radiances.reshape(-1, OBS_DEV, radiances.shape[1])

    def one_block(rows):
        return jnp.dot(rows, project_weight, preferred_element_type=jnp.float32).astype(jnp.bfloat16)
    return lax.map(one_block, blocks).reshape(-1, project_weight.shape[1])

def stride_conv(field, kernel):
    height, breadth, depth = field.shape
    upper_rim = jnp.zeros((1, breadth, depth), field.dtype)
    extended = jnp.concatenate([upper_rim, field], axis=0)
    padded = jnp.concatenate([extended[:, -1:], extended], axis=1)
    out_rows, out_cols = (height // 2, breadth // 2)
    summed = jnp.zeros((out_rows * out_cols, depth), jnp.float32)
    for row_tap in range(3):
        for col_tap in range(3):
            window = padded[row_tap:row_tap + 2 * out_rows:2, col_tap:col_tap + 2 * out_cols:2].reshape(-1, depth)
            summed = summed + jnp.dot(window, kernel[row_tap, col_tap], preferred_element_type=jnp.float32)
    return summed.reshape(out_rows, out_cols, depth)

def reference(radiances, project_weight, tile_ids, slot_offsets, tile_counts, setconv_weights, conv1_weight, conv2_weight):
    channel_count = project_weight.shape[1]
    features = project_rows(radiances, project_weight)
    tile_total = N_LAT * N_LON
    flat_block = jnp.zeros((tile_total * SLOTS, channel_count), jnp.bfloat16)
    flat_block = flat_block.at[(tile_ids * SLOTS + slot_offsets).astype(jnp.int32)].set(features)
    obs_block = flat_block.reshape(tile_total, SLOTS, channel_count)
    tile_weights = setconv_weights.reshape(N_LAT, CLAT, N_LON, CLON, SLOTS).transpose(0, 2, 1, 3, 4)
    tile_weights = tile_weights.reshape(tile_total, CLAT * CLON, SLOTS)
    counts_flat = tile_counts.reshape(-1).astype(jnp.int32)

    def one_tile(operands):
        weights_tile, block_tile, tile_count = operands
        live_mask = jnp.arange(SLOTS, dtype=jnp.int32) < tile_count
        masked = jnp.where(live_mask[None, :], weights_tile, jnp.zeros((), weights_tile.dtype))
        numerator = jnp.dot(masked, block_tile, preferred_element_type=jnp.float32)
        density = lax.optimization_barrier(jnp.sum(masked, axis=1, dtype=jnp.float32))
        return (numerator / jnp.sqrt(density)[:, None]).astype(jnp.bfloat16)
    tiles_out = lax.map(one_tile, (tile_weights, obs_block, counts_flat))
    grid = tiles_out.reshape(N_LAT, N_LON, CLAT, CLON, channel_count).transpose(0, 2, 1, 3, 4)
    grid = grid.reshape(NLAT, NLON, channel_count)
    hidden = jax.nn.gelu(stride_conv(grid, conv1_weight)).astype(jnp.bfloat16)
    return stride_conv(hidden, conv2_weight).astype(jnp.bfloat16)
```

```python
import jax
import jax.numpy as jnp
from jax import lax
from jax.sharding import PartitionSpec as P


def shifted_2(value, axis, by):
    peers = lax.axis_size(axis)
    pairs = [(i, i + by) for i in range(peers) if 0 <= i + by < peers]
    return lax.ppermute(value, axis, pairs)


def passed_along(value, axis, steps):
    count = lax.axis_size(axis)
    pairs = [(source, (source + steps) % count) for source in range(count)]
    return lax.ppermute(value, axis, pairs)


def diagonal(value):
    lat_size = lax.axis_size("lat")
    lon_size = lax.axis_size("lon")
    pairs = [
        (l * lon_size + n, (l + 1) * lon_size + (n + 1) % lon_size)
        for l in range(lat_size - 1)
        for n in range(lon_size)
    ]
    return lax.ppermute(value, ("lat", "lon"), pairs)


def stride_conv(field, kernel):
    height, breadth, depth = field.shape
    half_rows, half_cols = (height // 2, breadth // 2)
    upper_rim = shifted_2(field[-1:], "lat", 1)
    west_col = passed_along(field[:, -1:], "lon", 1)
    corner = diagonal(field[-1:, -1:])
    west_rim = jnp.concatenate([corner, west_col], axis=0)[:, 0]
    paired = field.reshape(half_rows, 2, half_cols, 2 * depth)
    even_rows = paired[:, 0]
    odd_rows = paired[:, 1]
    upper_paired = upper_rim.reshape(1, half_cols, 2 * depth)
    above_rows = jnp.concatenate([upper_paired, odd_rows[:-1]], axis=0)
    tap_rows = (above_rows, even_rows, odd_rows)
    zero_block = jnp.zeros((depth, depth), kernel.dtype)
    summed = jnp.zeros((half_rows * half_cols, 2 * depth), jnp.float32)
    west_sum = jnp.zeros((half_rows, depth), jnp.float32)
    for row_tap in range(3):
        upper_half = jnp.concatenate([kernel[row_tap, 1], zero_block], axis=1)
        lower_half = jnp.concatenate([kernel[row_tap, 2], kernel[row_tap, 0]], axis=1)
        stacked = jnp.concatenate([upper_half, lower_half], axis=0)
        rows_flat = tap_rows[row_tap].reshape(-1, 2 * depth)
        summed = summed + jnp.dot(rows_flat, stacked, preferred_element_type=jnp.float32)
        west_rows = west_rim[row_tap : row_tap + height : 2]
        west_sum = west_sum + jnp.dot(
            west_rows, kernel[row_tap, 0], preferred_element_type=jnp.float32
        )
    summed = summed.reshape(half_rows, half_cols, 2 * depth)
    central = summed[:, :, :depth]
    westward = summed[:, :, depth:]
    shifted = jnp.concatenate([west_sum[:, None, :], westward[:, :-1]], axis=1)
    return central + shifted


def body(
    radiances,
    project_weight,
    tile_ids,
    slot_offsets,
    tile_counts,
    setconv_weights,
    conv1_weight,
    conv2_weight,
):
    lat_size = lax.axis_size("lat")
    lon_size = lax.axis_size("lon")
    peer_count = lat_size * lon_size
    obs_count = radiances.shape[0]
    capacity = 7 * (obs_count // peer_count) // 2
    chunk_rows = ((capacity + 1 + 15) // 16) * 16
    slot_count = setconv_weights.shape[2]
    channel_count = project_weight.shape[1]
    digit = 64
    targets = jnp.arange(peer_count, dtype=jnp.int32)
    row_index = jnp.arange(obs_count, dtype=jnp.int32)
    matches = tile_ids[:, None] == targets[None, :]
    run_counts = jnp.sum(matches.astype(jnp.int32), axis=0)
    run_starts = jnp.min(jnp.where(matches, row_index[:, None], obs_count), axis=0)
    within = jnp.arange(capacity, dtype=jnp.int32)
    source_rows = (run_starts[:, None] + within[None, :]).reshape(-1)
    valid_slot = (within[None, :] < run_counts[:, None]).reshape(-1)
    selector = (
        (source_rows[:, None] == row_index[None, :]) & valid_slot[:, None]
    ).astype(jnp.bfloat16)
    payload = jnp.dot(radiances, project_weight, preferred_element_type=jnp.float32).astype(
        jnp.bfloat16
    )
    packed = jnp.dot(selector, payload, preferred_element_type=jnp.float32).astype(jnp.bfloat16)
    key = slot_offsets + 1
    digits = jnp.stack([key // digit, key % digit], axis=1).astype(jnp.bfloat16)
    packed_digits = jnp.dot(selector, digits, preferred_element_type=jnp.float32)
    packed_digits = packed_digits.reshape(peer_count, capacity, 2)
    digit_row = jnp.concatenate(
        [
            packed_digits[:, :, 0],
            packed_digits[:, :, 1],
            jnp.zeros((peer_count, channel_count - 2 * capacity), jnp.float32),
        ],
        axis=1,
    ).astype(jnp.bfloat16)
    outgoing = jnp.concatenate(
        [
            packed.reshape(peer_count, capacity, channel_count),
            digit_row[:, None, :],
            jnp.zeros((peer_count, chunk_rows - capacity - 1, channel_count), jnp.bfloat16),
        ],
        axis=1,
    )
    arrived = lax.all_to_all(outgoing, ("lat", "lon"), split_axis=0, concat_axis=0, tiled=True)
    arrived_rows = arrived[:, :capacity].reshape(-1, channel_count)
    arrived_digits = arrived[:, capacity].astype(jnp.int32)
    arrived_key = arrived_digits[:, :capacity] * digit + arrived_digits[:, capacity : 2 * capacity]
    arrived_offsets = arrived_key.reshape(-1) - 1
    slot_table = (
        jnp.arange(slot_count, dtype=jnp.int32)[:, None] == arrived_offsets[None, :]
    ).astype(jnp.bfloat16)
    obs_block = jnp.dot(slot_table, arrived_rows, preferred_element_type=jnp.float32).astype(
        jnp.bfloat16
    )
    tile_rows, tile_cols = (setconv_weights.shape[0], setconv_weights.shape[1])
    weights_flat = setconv_weights.reshape(-1, slot_count)
    live_mask = jnp.arange(slot_count, dtype=jnp.int32) < tile_counts.reshape(-1)[0]
    obs_masked = jnp.where(live_mask[:, None], obs_block, jnp.zeros((), jnp.bfloat16))
    numerator = jnp.dot(weights_flat, obs_masked, preferred_element_type=jnp.float32)
    masked = jnp.where(live_mask[None, :], weights_flat, jnp.zeros((), jnp.bfloat16))
    density = jnp.sum(masked, axis=1, dtype=jnp.float32)
    grid = (
        (numerator / jnp.sqrt(density)[:, None])
        .astype(jnp.bfloat16)
        .reshape(tile_rows, tile_cols, channel_count)
    )
    hidden = jax.nn.gelu(stride_conv(grid, conv1_weight)).astype(jnp.bfloat16)
    return stride_conv(hidden, conv2_weight).astype(jnp.bfloat16)


def solution(mesh):
    in_specs = (
        P(("lat", "lon"), None),
        P(),
        P(("lat", "lon")),
        P(("lat", "lon")),
        P("lat", "lon"),
        P("lat", "lon", None),
        P(),
        P(),
    )
    out_specs = P("lat", "lon", None)
    return jax.shard_map(body, mesh=mesh, in_specs=in_specs, out_specs=out_specs, check_vma=False)
```

```python
import jax
import jax.numpy as jnp
from jax import lax
from jax.sharding import PartitionSpec as P


def cyclic(value, axes, shifts):
    sizes = [lax.axis_size(a) for a in axes]
    pairs = []
    for l in range(sizes[0]):
        for n in range(sizes[-1] if len(axes) > 1 else 1):
            if len(axes) == 1:
                pairs.append((l, (l + shifts[0]) % sizes[0]))
            else:
                src = l * sizes[1] + n
                dst = ((l + shifts[0]) % sizes[0]) * sizes[1] + (n + shifts[1]) % sizes[1]
                pairs.append((src, dst))
    return lax.ppermute(value, axes if len(axes) > 1 else axes[0], pairs)


def strided_valid(field, kernel):
    height, breadth, depth = field.shape
    out_rows, out_cols = ((height - 3) // 2 + 1, (breadth - 3) // 2 + 1)
    summed = jnp.zeros((out_rows * out_cols, kernel.shape[3]), jnp.float32)
    for row_tap in range(3):
        for col_tap in range(3):
            window = lax.slice(
                field,
                (row_tap, col_tap, 0),
                (row_tap + 2 * out_rows - 1, col_tap + 2 * out_cols - 1, depth),
                (2, 2, 1),
            )
            summed = summed + jnp.dot(
                window.reshape(-1, depth),
                kernel[row_tap, col_tap],
                preferred_element_type=jnp.float32,
            )
    return summed.reshape(out_rows, out_cols, kernel.shape[3])


def encode_tile(grid, conv1_weight, conv2_weight):
    rim = 3
    north = cyclic(grid[-rim:], ("lat",), (1,))
    west = cyclic(grid[:, -rim:], ("lon",), (1,))
    north_west = cyclic(grid[-rim:, -rim:], ("lat", "lon"), (1, 1))
    top = jnp.concatenate([north_west, north], axis=1)
    top = jnp.where(lax.axis_index("lat") == 0, jnp.zeros((), top.dtype), top)
    body_rows = jnp.concatenate([west, grid], axis=1)
    extended = jnp.concatenate([top, body_rows], axis=0)
    hidden = jax.nn.gelu(strided_valid(extended, conv1_weight)).astype(jnp.bfloat16)
    return strided_valid(hidden, conv2_weight).astype(jnp.bfloat16)


def body(
    radiances,
    project_weight,
    tile_ids,
    slot_offsets,
    tile_counts,
    setconv_weights,
    conv1_weight,
    conv2_weight,
):
    lat_size = lax.axis_size("lat")
    lon_size = lax.axis_size("lon")
    peer_count = lat_size * lon_size
    obs_count = radiances.shape[0]
    capacity = 7 * (obs_count // peer_count) // 2
    chunk_rows = ((capacity + 1 + 15) // 16) * 16
    slot_count = setconv_weights.shape[2]
    channel_count = project_weight.shape[1]
    digit = 64
    targets = jnp.arange(peer_count, dtype=jnp.int32)
    row_index = jnp.arange(obs_count, dtype=jnp.int32)
    matches = tile_ids[:, None] == targets[None, :]
    run_counts = jnp.sum(matches.astype(jnp.int32), axis=0)
    run_starts = jnp.min(jnp.where(matches, row_index[:, None], obs_count), axis=0)
    within = jnp.arange(chunk_rows, dtype=jnp.int32)
    source_rows = (run_starts[:, None] + within[None, :]).reshape(-1)
    valid_slot = (
        (within[None, :] < run_counts[:, None]) & (within[None, :] < capacity)
    ).reshape(-1)
    selector = (
        (source_rows[:, None] == row_index[None, :]) & valid_slot[:, None]
    ).astype(jnp.bfloat16)
    payload = jnp.dot(radiances, project_weight, preferred_element_type=jnp.float32).astype(
        jnp.bfloat16
    )
    packed = jnp.dot(selector, payload, preferred_element_type=jnp.float32).astype(jnp.bfloat16)
    packed = packed.reshape(peer_count, chunk_rows, channel_count)
    key = jnp.concatenate([slot_offsets + 1, jnp.zeros((capacity,), jnp.int32)])
    hi_cols = jnp.stack([key[c : c + obs_count] // digit for c in range(capacity)], axis=1)
    lo_cols = jnp.stack([key[c : c + obs_count] % digit for c in range(capacity)], axis=1)
    windows = jnp.concatenate(
        [hi_cols, lo_cols, jnp.zeros((obs_count, channel_count - 2 * capacity), jnp.int32)],
        axis=1,
    ).astype(jnp.bfloat16)
    run_head = (run_starts[:, None] == row_index[None, :]).astype(jnp.bfloat16)
    digit_row = jnp.dot(run_head, windows, preferred_element_type=jnp.float32)
    column = jnp.arange(channel_count, dtype=jnp.int32)
    digit_live = (column[None, :] % capacity < run_counts[:, None]) & (
        column[None, :] < 2 * capacity
    )
    digit_row = jnp.where(digit_live, digit_row, 0.0).astype(jnp.bfloat16)
    outgoing = packed.at[:, capacity, :].set(digit_row)
    arrived = lax.all_to_all(outgoing, ("lat", "lon"), split_axis=0, concat_axis=0, tiled=True)
    arrived_rows = arrived[:, :capacity].reshape(-1, channel_count)
    arrived_digits = arrived[:, capacity].astype(jnp.int32)
    arrived_key = arrived_digits[:, :capacity] * digit + arrived_digits[:, capacity : 2 * capacity]
    arrived_offsets = arrived_key.reshape(-1) - 1
    slot_table = (
        jnp.arange(slot_count, dtype=jnp.int32)[:, None] == arrived_offsets[None, :]
    ).astype(jnp.bfloat16)
    obs_block = jnp.dot(slot_table, arrived_rows, preferred_element_type=jnp.float32).astype(
        jnp.bfloat16
    )
    tile_rows, tile_cols = (setconv_weights.shape[0], setconv_weights.shape[1])
    weights_flat = setconv_weights.reshape(-1, slot_count)
    live_mask = jnp.arange(slot_count, dtype=jnp.int32) < tile_counts.reshape(-1)[0]
    obs_masked = jnp.where(live_mask[:, None], obs_block, jnp.zeros((), jnp.bfloat16))
    numerator = jnp.dot(weights_flat, obs_masked, preferred_element_type=jnp.float32)
    masked = jnp.where(live_mask[None, :], weights_flat, jnp.zeros((), jnp.bfloat16))
    density = jnp.sum(masked, axis=1, dtype=jnp.float32)
    grid = (
        (numerator / jnp.sqrt(density)[:, None])
        .astype(jnp.bfloat16)
        .reshape(tile_rows, tile_cols, channel_count)
    )
    return encode_tile(grid, conv1_weight, conv2_weight)


def solution(mesh):
    in_specs = (
        P(("lat", "lon"), None),
        P(),
        P(("lat", "lon")),
        P(("lat", "lon")),
        P("lat", "lon"),
        P("lat", "lon", None),
        P(),
        P(),
    )
    out_specs = P("lat", "lon", None)
    return jax.shard_map(body, mesh=mesh, in_specs=in_specs, out_specs=out_specs, check_vma=False)
```

```python
import jax
import jax.numpy as jnp
from jax import lax
from jax.sharding import PartitionSpec as P


def cyclic(value, axes, shifts):
    sizes = [lax.axis_size(a) for a in axes]
    pairs = []
    for l in range(sizes[0]):
        for n in range(sizes[-1] if len(axes) > 1 else 1):
            if len(axes) == 1:
                pairs.append((l, (l + shifts[0]) % sizes[0]))
            else:
                src = l * sizes[1] + n
                dst = ((l + shifts[0]) % sizes[0]) * sizes[1] + (n + shifts[1]) % sizes[1]
                pairs.append((src, dst))
    return lax.ppermute(value, axes if len(axes) > 1 else axes[0], pairs)


def strided_valid(field, kernel):
    height, breadth, depth = field.shape
    out_rows, out_cols = ((height - 3) // 2 + 1, (breadth - 3) // 2 + 1)
    even_h, even_w = (height + height % 2, breadth + breadth % 2)
    padded = jnp.pad(field, ((0, even_h - height), (0, even_w - breadth), (0, 0)))
    pairs = padded.reshape(even_h // 2, 2, even_w // 2, 2 * depth)
    zero_block = jnp.zeros((depth, depth), kernel.dtype)
    near = jnp.zeros((out_rows * (even_w // 2), depth), jnp.float32)
    far = jnp.zeros((out_rows * (even_w // 2), depth), jnp.float32)
    for row_tap in range(3):
        rows = pairs[row_tap // 2 : row_tap // 2 + out_rows, row_tap % 2]
        stacked = jnp.concatenate(
            [
                jnp.concatenate([kernel[row_tap, 0], kernel[row_tap, 2]], axis=1),
                jnp.concatenate([kernel[row_tap, 1], zero_block], axis=1),
            ],
            axis=0,
        )
        both = jnp.dot(rows.reshape(-1, 2 * depth), stacked, preferred_element_type=jnp.float32)
        near = near + both[:, :depth]
        far = far + both[:, depth:]
    near = near.reshape(out_rows, even_w // 2, depth)
    far = far.reshape(out_rows, even_w // 2, depth)
    return near[:, :out_cols] + far[:, 1 : out_cols + 1]


def encode_tile(grid, conv1_weight, conv2_weight):
    rim = 3
    north = cyclic(grid[-rim:], ("lat",), (1,))
    west = cyclic(grid[:, -rim:], ("lon",), (1,))
    north_west = cyclic(grid[-rim:, -rim:], ("lat", "lon"), (1, 1))
    top = jnp.concatenate([north_west, north], axis=1)
    top = jnp.where(lax.axis_index("lat") == 0, jnp.zeros((), top.dtype), top)
    body_rows = jnp.concatenate([west, grid], axis=1)
    extended = jnp.concatenate([top, body_rows], axis=0)
    hidden = jax.nn.gelu(strided_valid(extended, conv1_weight)).astype(jnp.bfloat16)
    return strided_valid(hidden, conv2_weight).astype(jnp.bfloat16)


def body(
    radiances,
    project_weight,
    tile_ids,
    slot_offsets,
    tile_counts,
    setconv_weights,
    conv1_weight,
    conv2_weight,
):
    lat_size = lax.axis_size("lat")
    lon_size = lax.axis_size("lon")
    peer_count = lat_size * lon_size
    obs_count = radiances.shape[0]
    capacity = 7 * (obs_count // peer_count) // 2
    chunk_rows = ((capacity + 1 + 15) // 16) * 16
    slot_count = setconv_weights.shape[2]
    channel_count = project_weight.shape[1]
    digit = 64
    targets = jnp.arange(peer_count, dtype=jnp.int32)
    row_index = jnp.arange(obs_count, dtype=jnp.int32)
    matches = tile_ids[:, None] == targets[None, :]
    run_counts = jnp.sum(matches.astype(jnp.int32), axis=0)
    run_starts = jnp.min(jnp.where(matches, row_index[:, None], obs_count), axis=0)
    within = jnp.arange(chunk_rows, dtype=jnp.int32)
    source_rows = (run_starts[:, None] + within[None, :]).reshape(-1)
    valid_slot = (
        (within[None, :] < run_counts[:, None]) & (within[None, :] < capacity)
    ).reshape(-1)
    selector = (
        (source_rows[:, None] == row_index[None, :]) & valid_slot[:, None]
    ).astype(jnp.bfloat16)
    payload = jnp.dot(radiances, project_weight, preferred_element_type=jnp.float32).astype(
        jnp.bfloat16
    )
    packed = jnp.dot(selector, payload, preferred_element_type=jnp.float32).astype(jnp.bfloat16)
    packed = packed.reshape(peer_count, chunk_rows, channel_count)
    key = slot_offsets + 1
    digits = jnp.stack([key // digit, key % digit], axis=1).astype(jnp.bfloat16)
    packed_digits = jnp.dot(selector, digits, preferred_element_type=jnp.float32)
    packed_digits = packed_digits.reshape(peer_count, chunk_rows, 2)[:, :capacity]
    digit_row = jnp.concatenate(
        [
            packed_digits[:, :, 0],
            packed_digits[:, :, 1],
            jnp.zeros((peer_count, channel_count - 2 * capacity), jnp.float32),
        ],
        axis=1,
    ).astype(jnp.bfloat16)
    outgoing = lax.dynamic_update_slice(packed, digit_row[:, None, :], (0, capacity, 0))
    arrived = lax.all_to_all(outgoing, ("lat", "lon"), split_axis=0, concat_axis=0, tiled=True)
    arrived_rows = arrived[:, :capacity].reshape(-1, channel_count)
    arrived_digits = arrived[:, capacity].astype(jnp.int32)
    arrived_key = arrived_digits[:, :capacity] * digit + arrived_digits[:, capacity : 2 * capacity]
    arrived_offsets = arrived_key.reshape(-1) - 1
    slot_table = (
        jnp.arange(slot_count, dtype=jnp.int32)[:, None] == arrived_offsets[None, :]
    ).astype(jnp.bfloat16)
    obs_block = jnp.dot(slot_table, arrived_rows, preferred_element_type=jnp.float32).astype(
        jnp.bfloat16
    )
    tile_rows, tile_cols = (setconv_weights.shape[0], setconv_weights.shape[1])
    weights_flat = setconv_weights.reshape(-1, slot_count)
    live_mask = jnp.arange(slot_count, dtype=jnp.int32) < tile_counts.reshape(-1)[0]
    obs_masked = jnp.where(live_mask[:, None], obs_block, jnp.zeros((), jnp.bfloat16))
    numerator = jnp.dot(weights_flat, obs_masked, preferred_element_type=jnp.float32)
    masked = jnp.where(live_mask[None, :], weights_flat, jnp.zeros((), jnp.bfloat16))
    density = jnp.sum(masked, axis=1, dtype=jnp.float32)
    grid = (
        (numerator / jnp.sqrt(density)[:, None])
        .astype(jnp.bfloat16)
        .reshape(tile_rows, tile_cols, channel_count)
    )
    return encode_tile(grid, conv1_weight, conv2_weight)


def solution(mesh):
    in_specs = (
        P(("lat", "lon"), None),
        P(),
        P(("lat", "lon")),
        P(("lat", "lon")),
        P("lat", "lon"),
        P("lat", "lon", None),
        P(),
        P(),
    )
    out_specs = P("lat", "lon", None)
    return jax.shard_map(body, mesh=mesh, in_specs=in_specs, out_specs=out_specs, check_vma=False)
```

```python
import jax
import jax.numpy as jnp
from jax import lax
from jax.sharding import PartitionSpec as P


def cyclic(value, axes, shifts):
    sizes = [lax.axis_size(a) for a in axes]
    pairs = []
    for l in range(sizes[0]):
        for n in range(sizes[-1] if len(axes) > 1 else 1):
            if len(axes) == 1:
                pairs.append((l, (l + shifts[0]) % sizes[0]))
            else:
                src = l * sizes[1] + n
                dst = ((l + shifts[0]) % sizes[0]) * sizes[1] + (n + shifts[1]) % sizes[1]
                pairs.append((src, dst))
    return lax.ppermute(value, axes if len(axes) > 1 else axes[0], pairs)


def strided_valid(field, kernel):
    height, breadth, depth = field.shape
    out_rows, out_cols = ((height - 3) // 2 + 1, (breadth - 3) // 2 + 1)
    even_h, even_w = (height + height % 2, breadth + breadth % 2)
    padded = jnp.pad(field, ((0, even_h - height), (0, even_w - breadth), (0, 0)))
    pairs = padded.reshape(even_h // 2, 2, even_w // 2, 2 * depth)
    zero_block = jnp.zeros((depth, depth), kernel.dtype)
    near = jnp.zeros((out_rows * (even_w // 2), depth), jnp.float32)
    far = jnp.zeros((out_rows * (even_w // 2), depth), jnp.float32)
    for row_tap in range(3):
        rows = pairs[row_tap // 2 : row_tap // 2 + out_rows, row_tap % 2]
        stacked = jnp.concatenate(
            [
                jnp.concatenate([kernel[row_tap, 0], kernel[row_tap, 2]], axis=1),
                jnp.concatenate([kernel[row_tap, 1], zero_block], axis=1),
            ],
            axis=0,
        )
        both = jnp.dot(rows.reshape(-1, 2 * depth), stacked, preferred_element_type=jnp.float32)
        near = near + both[:, :depth]
        far = far + both[:, depth:]
    near = near.reshape(out_rows, even_w // 2, depth)
    far = far.reshape(out_rows, even_w // 2, depth)
    return near[:, :out_cols] + far[:, 1 : out_cols + 1]


def encode_tile(grid, north, west, north_west, conv1_weight, conv2_weight):
    top = jnp.concatenate([north_west, north], axis=1)
    top = jnp.where(lax.axis_index("lat") == 0, jnp.zeros((), top.dtype), top)
    body_rows = jnp.concatenate([west, grid], axis=1)
    extended = jnp.concatenate([top, body_rows], axis=0)
    hidden = jax.nn.gelu(strided_valid(extended, conv1_weight)).astype(jnp.bfloat16)
    return strided_valid(hidden, conv2_weight).astype(jnp.bfloat16)


def body(
    radiances,
    project_weight,
    tile_ids,
    slot_offsets,
    tile_counts,
    setconv_weights,
    conv1_weight,
    conv2_weight,
):
    lat_size = lax.axis_size("lat")
    lon_size = lax.axis_size("lon")
    peer_count = lat_size * lon_size
    obs_count = radiances.shape[0]
    capacity = 7 * (obs_count // peer_count) // 2
    chunk_rows = ((capacity + 1 + 15) // 16) * 16
    slot_count = setconv_weights.shape[2]
    channel_count = project_weight.shape[1]
    digit = 64
    targets = jnp.arange(peer_count, dtype=jnp.int32)
    row_index = jnp.arange(obs_count, dtype=jnp.int32)
    matches = tile_ids[:, None] == targets[None, :]
    run_counts = jnp.sum(matches.astype(jnp.int32), axis=0)
    run_starts = jnp.min(jnp.where(matches, row_index[:, None], obs_count), axis=0)
    within = jnp.arange(chunk_rows, dtype=jnp.int32)
    source_rows = (run_starts[:, None] + within[None, :]).reshape(-1)
    valid_slot = (
        (within[None, :] < run_counts[:, None]) & (within[None, :] < capacity)
    ).reshape(-1)
    selector = (
        (source_rows[:, None] == row_index[None, :]) & valid_slot[:, None]
    ).astype(jnp.bfloat16)
    payload = jnp.dot(radiances, project_weight, preferred_element_type=jnp.float32).astype(
        jnp.bfloat16
    )
    key = slot_offsets + 1
    digits = jnp.stack([key // digit, key % digit], axis=1).astype(jnp.bfloat16)
    packed_digits = jnp.dot(selector, digits, preferred_element_type=jnp.float32)
    packed_digits = packed_digits.reshape(peer_count, chunk_rows, 2)[:, :capacity]
    digit_row = jnp.concatenate(
        [
            packed_digits[:, :, 0],
            packed_digits[:, :, 1],
            jnp.zeros((peer_count, channel_count - 2 * capacity), jnp.float32),
        ],
        axis=1,
    ).astype(jnp.bfloat16)
    chunk_of = jnp.repeat(targets, chunk_rows)
    row_of = jnp.tile(within, peer_count)
    digit_pick = (row_of[:, None] == capacity) & (chunk_of[:, None] == targets[None, :])
    selector_all = jnp.concatenate([selector, digit_pick.astype(jnp.bfloat16)], axis=1)
    sources = jnp.concatenate([payload, digit_row], axis=0)
    outgoing = jnp.dot(selector_all, sources, preferred_element_type=jnp.float32).astype(
        jnp.bfloat16
    )
    outgoing = outgoing.reshape(peer_count, chunk_rows, channel_count)
    arrived = lax.all_to_all(outgoing, ("lat", "lon"), split_axis=0, concat_axis=0, tiled=True)
    arrived_rows = arrived[:, :capacity].reshape(-1, channel_count)
    arrived_digits = arrived[:, capacity].astype(jnp.int32)
    arrived_key = arrived_digits[:, :capacity] * digit + arrived_digits[:, capacity : 2 * capacity]
    arrived_offsets = arrived_key.reshape(-1) - 1
    slot_table = (
        jnp.arange(slot_count, dtype=jnp.int32)[:, None] == arrived_offsets[None, :]
    ).astype(jnp.bfloat16)
    obs_block = jnp.dot(slot_table, arrived_rows, preferred_element_type=jnp.float32).astype(
        jnp.bfloat16
    )
    tile_rows, tile_cols = (setconv_weights.shape[0], setconv_weights.shape[1])
    weights_flat = setconv_weights.reshape(-1, slot_count)
    live_mask = jnp.arange(slot_count, dtype=jnp.int32) < tile_counts.reshape(-1)[0]
    obs_masked = jnp.where(live_mask[:, None], obs_block, jnp.zeros((), jnp.bfloat16))
    masked = jnp.where(live_mask[None, :], weights_flat, jnp.zeros((), jnp.bfloat16))
    density = jnp.sum(masked, axis=1, dtype=jnp.float32)
    root = jnp.sqrt(density).reshape(tile_rows, tile_cols, 1)
    weights_cells = setconv_weights

    def cells(weights, roots):
        shape = weights.shape[:-1]
        numer = jnp.dot(weights.reshape(-1, slot_count), obs_masked, preferred_element_type=jnp.float32)
        return (numer.reshape(shape + (channel_count,)) / roots).astype(jnp.bfloat16)

    rim = 3
    rim_weights = jnp.concatenate(
        [
            weights_cells[-rim:].reshape(-1, slot_count),
            weights_cells[:, -rim:].reshape(-1, slot_count),
        ],
        axis=0,
    )
    rim_roots = jnp.concatenate([root[-rim:].reshape(-1, 1), root[:, -rim:].reshape(-1, 1)], axis=0)
    rim_cells = cells(rim_weights, rim_roots)
    north_rows = rim_cells[: rim * tile_cols].reshape(rim, tile_cols, channel_count)
    west_cols = rim_cells[rim * tile_cols :].reshape(tile_rows, rim, channel_count)
    north = cyclic(north_rows, ("lat",), (1,))
    west = cyclic(west_cols, ("lon",), (1,))
    north_west = cyclic(north_rows[:, -rim:], ("lat", "lon"), (1, 1))
    grid = cells(weights_cells, root)
    return encode_tile(grid, north, west, north_west, conv1_weight, conv2_weight)


def solution(mesh):
    in_specs = (
        P(("lat", "lon"), None),
        P(),
        P(("lat", "lon")),
        P(("lat", "lon")),
        P("lat", "lon"),
        P("lat", "lon", None),
        P(),
        P(),
    )
    out_specs = P("lat", "lon", None)
    return jax.shard_map(body, mesh=mesh, in_specs=in_specs, out_specs=out_specs, check_vma=False)
```

```python
import jax
import jax.numpy as jnp
from jax import lax
from jax.sharding import PartitionSpec as P


def cyclic(value, axes, shifts):
    sizes = [lax.axis_size(a) for a in axes]
    pairs = []
    for l in range(sizes[0]):
        for n in range(sizes[-1] if len(axes) > 1 else 1):
            if len(axes) == 1:
                pairs.append((l, (l + shifts[0]) % sizes[0]))
            else:
                src = l * sizes[1] + n
                dst = ((l + shifts[0]) % sizes[0]) * sizes[1] + (n + shifts[1]) % sizes[1]
                pairs.append((src, dst))
    return lax.ppermute(value, axes if len(axes) > 1 else axes[0], pairs)


def strided_valid(field, kernel):
    height, breadth, depth = field.shape
    out_rows, out_cols = ((height - 3) // 2 + 1, (breadth - 3) // 2 + 1)
    even_h, even_w = (height + height % 2, breadth + breadth % 2)
    padded = jnp.pad(field, ((0, even_h - height), (0, even_w - breadth), (0, 0)))
    pairs = padded.reshape(even_h // 2, 2, even_w // 2, 2 * depth)
    zero_block = jnp.zeros((depth, depth), kernel.dtype)
    near = jnp.zeros((out_rows * (even_w // 2), depth), jnp.float32)
    far = jnp.zeros((out_rows * (even_w // 2), depth), jnp.float32)
    for row_tap in range(3):
        rows = pairs[row_tap // 2 : row_tap // 2 + out_rows, row_tap % 2]
        stacked = jnp.concatenate(
            [
                jnp.concatenate([kernel[row_tap, 0], kernel[row_tap, 2]], axis=1),
                jnp.concatenate([kernel[row_tap, 1], zero_block], axis=1),
            ],
            axis=0,
        )
        both = jnp.dot(rows.reshape(-1, 2 * depth), stacked, preferred_element_type=jnp.float32)
        near = near + both[:, :depth]
        far = far + both[:, depth:]
    near = near.reshape(out_rows, even_w // 2, depth)
    far = far.reshape(out_rows, even_w // 2, depth)
    return near[:, :out_cols] + far[:, 1 : out_cols + 1]


def encode_tile(grid, north, west, north_west, conv1_weight, conv2_weight):
    top = jnp.concatenate([north_west, north], axis=1)
    top = jnp.where(lax.axis_index("lat") == 0, jnp.zeros((), top.dtype), top)
    body_rows = jnp.concatenate([west, grid], axis=1)
    extended = jnp.concatenate([top, body_rows], axis=0)
    hidden = jax.nn.gelu(strided_valid(extended, conv1_weight)).astype(jnp.bfloat16)
    return strided_valid(hidden, conv2_weight).astype(jnp.bfloat16)


def body(
    radiances,
    project_weight,
    tile_ids,
    slot_offsets,
    tile_counts,
    setconv_weights,
    conv1_weight,
    conv2_weight,
):
    lat_size = lax.axis_size("lat")
    lon_size = lax.axis_size("lon")
    peer_count = lat_size * lon_size
    obs_count = radiances.shape[0]
    capacity = 7 * (obs_count // peer_count) // 2
    chunk_rows = ((capacity + 1 + 15) // 16) * 16
    slot_count = setconv_weights.shape[2]
    channel_count = project_weight.shape[1]
    digit = 64
    targets = jnp.arange(peer_count, dtype=jnp.int32)
    row_index = jnp.arange(obs_count, dtype=jnp.int32)
    matches = tile_ids[:, None] == targets[None, :]
    run_counts = jnp.sum(matches.astype(jnp.int32), axis=0)
    run_starts = jnp.min(jnp.where(matches, row_index[:, None], obs_count), axis=0)
    within = jnp.arange(chunk_rows, dtype=jnp.int32)
    source_rows = (run_starts[:, None] + within[None, :]).reshape(-1)
    valid_slot = (
        (within[None, :] < run_counts[:, None]) & (within[None, :] < capacity)
    ).reshape(-1)
    selector = (
        (source_rows[:, None] == row_index[None, :]) & valid_slot[:, None]
    ).astype(jnp.bfloat16)
    payload = jnp.dot(radiances, project_weight, preferred_element_type=jnp.float32).astype(
        jnp.bfloat16
    )
    key = slot_offsets + 1
    period = obs_count + 2 * capacity
    key_ext = jnp.concatenate([key, jnp.zeros((period - obs_count,), jnp.int32)])
    tiled_keys = jnp.tile(key_ext, capacity + 1)[: capacity * (period + 1)]
    hankel = tiled_keys.reshape(capacity, period + 1)[:, :obs_count].T
    windows = jnp.concatenate(
        [
            hankel // digit,
            hankel % digit,
            jnp.zeros((obs_count, channel_count - 2 * capacity), jnp.int32),
        ],
        axis=1,
    ).astype(jnp.bfloat16)
    run_head = (run_starts[:, None] == row_index[None, :]).astype(jnp.bfloat16)
    digit_row = jnp.dot(run_head, windows, preferred_element_type=jnp.float32)
    column = jnp.arange(channel_count, dtype=jnp.int32)
    digit_live = (column[None, :] % capacity < run_counts[:, None]) & (
        column[None, :] < 2 * capacity
    )
    digit_row = jnp.where(digit_live, digit_row, 0.0).astype(jnp.bfloat16)
    chunk_of = jnp.repeat(targets, chunk_rows)
    row_of = jnp.tile(within, peer_count)
    digit_pick = (row_of[:, None] == capacity) & (chunk_of[:, None] == targets[None, :])
    selector_all = jnp.concatenate([selector, digit_pick.astype(jnp.bfloat16)], axis=1)
    sources = jnp.concatenate([payload, digit_row], axis=0)
    outgoing = jnp.dot(selector_all, sources, preferred_element_type=jnp.float32).astype(
        jnp.bfloat16
    )
    outgoing = outgoing.reshape(peer_count, chunk_rows, channel_count)
    arrived = lax.all_to_all(outgoing, ("lat", "lon"), split_axis=0, concat_axis=0, tiled=True)
    arrived_rows = arrived[:, :capacity].reshape(-1, channel_count)
    arrived_digits = arrived[:, capacity].astype(jnp.int32)
    arrived_key = arrived_digits[:, :capacity] * digit + arrived_digits[:, capacity : 2 * capacity]
    arrived_offsets = arrived_key.reshape(-1) - 1
    slot_table = (
        jnp.arange(slot_count, dtype=jnp.int32)[:, None] == arrived_offsets[None, :]
    ).astype(jnp.bfloat16)
    obs_block = jnp.dot(slot_table, arrived_rows, preferred_element_type=jnp.float32).astype(
        jnp.bfloat16
    )
    tile_rows, tile_cols = (setconv_weights.shape[0], setconv_weights.shape[1])
    weights_flat = setconv_weights.reshape(-1, slot_count)
    live_mask = jnp.arange(slot_count, dtype=jnp.int32) < tile_counts.reshape(-1)[0]
    obs_masked = jnp.where(live_mask[:, None], obs_block, jnp.zeros((), jnp.bfloat16))
    masked = jnp.where(live_mask[None, :], weights_flat, jnp.zeros((), jnp.bfloat16))
    density = jnp.sum(masked, axis=1, dtype=jnp.float32)
    root = jnp.sqrt(density).reshape(tile_rows, tile_cols, 1)
    weights_cells = setconv_weights

    def cells(weights, roots):
        numer = jnp.dot(weights, obs_masked, preferred_element_type=jnp.float32)
        return (numer / roots).astype(jnp.bfloat16)

    rim = 3
    rim_weights = jnp.concatenate(
        [
            weights_cells[-rim:].reshape(-1, slot_count),
            weights_cells[:, -rim:].reshape(-1, slot_count),
        ],
        axis=0,
    )
    rim_roots = jnp.concatenate([root[-rim:].reshape(-1, 1), root[:, -rim:].reshape(-1, 1)], axis=0)
    rim_cells = cells(rim_weights, rim_roots)
    north_rows = rim_cells[: rim * tile_cols].reshape(rim, tile_cols, channel_count)
    west_cols = rim_cells[rim * tile_cols :].reshape(tile_rows, rim, channel_count)
    north = cyclic(north_rows, ("lat",), (1,))
    west = cyclic(west_cols, ("lon",), (1,))
    north_west = cyclic(north_rows[:, -rim:], ("lat", "lon"), (1, 1))
    grid = cells(weights_flat, root.reshape(-1, 1)).reshape(tile_rows, tile_cols, channel_count)
    return encode_tile(grid, north, west, north_west, conv1_weight, conv2_weight)


def solution(mesh):
    in_specs = (
        P(("lat", "lon"), None),
        P(),
        P(("lat", "lon")),
        P(("lat", "lon")),
        P("lat", "lon"),
        P("lat", "lon", None),
        P(),
        P(),
    )
    out_specs = P("lat", "lon", None)
    return jax.shard_map(body, mesh=mesh, in_specs=in_specs, out_specs=out_specs, check_vma=False)
```

```python
import jax
import jax.numpy as jnp
from jax import lax
from jax.sharding import PartitionSpec as P


def cyclic(value, axes, shifts):
    sizes = [lax.axis_size(a) for a in axes]
    pairs = []
    for l in range(sizes[0]):
        for n in range(sizes[-1] if len(axes) > 1 else 1):
            if len(axes) == 1:
                pairs.append((l, (l + shifts[0]) % sizes[0]))
            else:
                src = l * sizes[1] + n
                dst = ((l + shifts[0]) % sizes[0]) * sizes[1] + (n + shifts[1]) % sizes[1]
                pairs.append((src, dst))
    return lax.ppermute(value, axes if len(axes) > 1 else axes[0], pairs)


def strided_valid(field, kernel):
    height, breadth, depth = field.shape
    out_rows, out_cols = ((height - 3) // 2 + 1, (breadth - 3) // 2 + 1)
    even_h, even_w = (height + height % 2, breadth + breadth % 2)
    padded = jnp.pad(field, ((0, even_h - height), (0, even_w - breadth), (0, 0)))
    pairs = padded.reshape(even_h // 2, 2, even_w // 2, 2 * depth)
    zero_block = jnp.zeros((depth, depth), kernel.dtype)
    near = jnp.zeros((out_rows * (even_w // 2), depth), jnp.float32)
    far = jnp.zeros((out_rows * (even_w // 2), depth), jnp.float32)
    for row_tap in range(3):
        rows = pairs[row_tap // 2 : row_tap // 2 + out_rows, row_tap % 2]
        stacked = jnp.concatenate(
            [
                jnp.concatenate([kernel[row_tap, 0], kernel[row_tap, 2]], axis=1),
                jnp.concatenate([kernel[row_tap, 1], zero_block], axis=1),
            ],
            axis=0,
        )
        both = jnp.dot(rows.reshape(-1, 2 * depth), stacked, preferred_element_type=jnp.float32)
        near = near + both[:, :depth]
        far = far + both[:, depth:]
    near = near.reshape(out_rows, even_w // 2, depth)
    far = far.reshape(out_rows, even_w // 2, depth)
    return near[:, :out_cols] + far[:, 1 : out_cols + 1]


def encode_tile(grid, north, west, north_west, conv1_weight, conv2_weight):
    top = jnp.concatenate([north_west, north], axis=1)
    top = jnp.where(lax.axis_index("lat") == 0, jnp.zeros((), top.dtype), top)
    body_rows = jnp.concatenate([west, grid], axis=1)
    extended = jnp.concatenate([top, body_rows], axis=0)
    hidden = jax.nn.gelu(strided_valid(extended, conv1_weight)).astype(jnp.bfloat16)
    return strided_valid(hidden, conv2_weight).astype(jnp.bfloat16)


def body(
    radiances,
    project_weight,
    tile_ids,
    slot_offsets,
    tile_counts,
    setconv_weights,
    conv1_weight,
    conv2_weight,
):
    lat_size = lax.axis_size("lat")
    lon_size = lax.axis_size("lon")
    peer_count = lat_size * lon_size
    obs_count = radiances.shape[0]
    capacity = 7 * (obs_count // peer_count) // 2
    chunk_rows = ((capacity + 1 + 15) // 16) * 16
    slot_count = setconv_weights.shape[2]
    channel_count = project_weight.shape[1]
    digit = 64
    targets = jnp.arange(peer_count, dtype=jnp.int32)
    row_index = jnp.arange(obs_count, dtype=jnp.int32)
    matches = tile_ids[:, None] == targets[None, :]
    run_counts = jnp.sum(matches.astype(jnp.int32), axis=0)
    run_starts = jnp.min(jnp.where(matches, row_index[:, None], obs_count), axis=0)
    within = jnp.arange(chunk_rows, dtype=jnp.int32)
    source_rows = (run_starts[:, None] + within[None, :]).reshape(-1)
    valid_slot = (
        (within[None, :] < run_counts[:, None]) & (within[None, :] < capacity)
    ).reshape(-1)
    selector = (
        (source_rows[:, None] == row_index[None, :]) & valid_slot[:, None]
    ).astype(jnp.bfloat16)
    payload = jnp.dot(radiances, project_weight, preferred_element_type=jnp.float32).astype(
        jnp.bfloat16
    )
    key = slot_offsets + 1
    period = obs_count + 2 * capacity
    key_ext = jnp.concatenate([key, jnp.zeros((period - obs_count,), jnp.int32)])
    tiled_keys = jnp.tile(key_ext, capacity + 1)[: capacity * (period + 1)]
    hankel = tiled_keys.reshape(capacity, period + 1)[:, :obs_count].T
    windows = jnp.concatenate(
        [
            hankel // digit,
            hankel % digit,
            jnp.zeros((obs_count, channel_count - 2 * capacity), jnp.int32),
        ],
        axis=1,
    ).astype(jnp.bfloat16)
    run_head = (run_starts[:, None] == row_index[None, :]).astype(jnp.bfloat16)
    digit_row = jnp.dot(run_head, windows, preferred_element_type=jnp.float32)
    column = jnp.arange(channel_count, dtype=jnp.int32)
    digit_live = (column[None, :] % capacity < run_counts[:, None]) & (
        column[None, :] < 2 * capacity
    )
    digit_row = jnp.where(digit_live, digit_row, 0.0).astype(jnp.bfloat16)
    packed = jnp.dot(selector, payload, preferred_element_type=jnp.float32).astype(jnp.bfloat16)
    packed = packed.reshape(peer_count, chunk_rows, channel_count)
    outgoing = jnp.where(
        (within == capacity)[None, :, None], digit_row[:, None, :], packed
    )
    arrived = lax.all_to_all(outgoing, ("lat", "lon"), split_axis=0, concat_axis=0, tiled=True)
    arrived_rows = arrived[:, :capacity].reshape(-1, channel_count)
    arrived_digits = arrived[:, capacity].astype(jnp.int32)
    arrived_key = arrived_digits[:, :capacity] * digit + arrived_digits[:, capacity : 2 * capacity]
    arrived_offsets = arrived_key.reshape(-1) - 1
    slot_table = (
        jnp.arange(slot_count, dtype=jnp.int32)[:, None] == arrived_offsets[None, :]
    ).astype(jnp.bfloat16)
    obs_block = jnp.dot(slot_table, arrived_rows, preferred_element_type=jnp.float32).astype(
        jnp.bfloat16
    )
    tile_rows, tile_cols = (setconv_weights.shape[0], setconv_weights.shape[1])
    weights_flat = setconv_weights.reshape(-1, slot_count)
    live_mask = jnp.arange(slot_count, dtype=jnp.int32) < tile_counts.reshape(-1)[0]
    obs_masked = jnp.where(live_mask[:, None], obs_block, jnp.zeros((), jnp.bfloat16))
    masked = jnp.where(live_mask[None, :], weights_flat, jnp.zeros((), jnp.bfloat16))
    density = jnp.sum(masked, axis=1, dtype=jnp.float32)
    root = jnp.sqrt(density).reshape(tile_rows, tile_cols, 1)
    weights_cells = setconv_weights

    def cells(weights, roots):
        numer = jnp.dot(weights, obs_masked, preferred_element_type=jnp.float32)
        return (numer / roots).astype(jnp.bfloat16)

    rim = 3
    rim_weights = jnp.concatenate(
        [
            weights_cells[-rim:].reshape(-1, slot_count),
            weights_cells[:, -rim:].reshape(-1, slot_count),
        ],
        axis=0,
    )
    rim_roots = jnp.concatenate([root[-rim:].reshape(-1, 1), root[:, -rim:].reshape(-1, 1)], axis=0)
    rim_cells = cells(rim_weights, rim_roots)
    north_rows = rim_cells[: rim * tile_cols].reshape(rim, tile_cols, channel_count)
    west_cols = rim_cells[rim * tile_cols :].reshape(tile_rows, rim, channel_count)
    north = cyclic(north_rows, ("lat",), (1,))
    west = cyclic(west_cols, ("lon",), (1,))
    north_west = cyclic(north_rows[:, -rim:], ("lat", "lon"), (1, 1))
    grid = cells(weights_flat, root.reshape(-1, 1)).reshape(tile_rows, tile_cols, channel_count)
    return encode_tile(grid, north, west, north_west, conv1_weight, conv2_weight)


def solution(mesh):
    in_specs = (
        P(("lat", "lon"), None),
        P(),
        P(("lat", "lon")),
        P(("lat", "lon")),
        P("lat", "lon"),
        P("lat", "lon", None),
        P(),
        P(),
    )
    out_specs = P("lat", "lon", None)
    return jax.shard_map(body, mesh=mesh, in_specs=in_specs, out_specs=out_specs, check_vma=False)
```

```python
import jax
import jax.numpy as jnp
from jax import lax
from jax.sharding import PartitionSpec as P


def cyclic(value, axes, shifts):
    sizes = [lax.axis_size(a) for a in axes]
    pairs = []
    for l in range(sizes[0]):
        for n in range(sizes[-1] if len(axes) > 1 else 1):
            if len(axes) == 1:
                pairs.append((l, (l + shifts[0]) % sizes[0]))
            else:
                src = l * sizes[1] + n
                dst = ((l + shifts[0]) % sizes[0]) * sizes[1] + (n + shifts[1]) % sizes[1]
                pairs.append((src, dst))
    return lax.ppermute(value, axes if len(axes) > 1 else axes[0], pairs)


def strided_valid(field, kernel):
    height, breadth, depth = field.shape
    out_rows, out_cols = ((height - 3) // 2 + 1, (breadth - 3) // 2 + 1)
    even_h, even_w = (height + height % 2, -(-breadth // 32) * 32)
    padded = jnp.pad(field, ((0, even_h - height), (0, even_w - breadth), (0, 0)))
    pairs = padded.reshape(even_h // 2, 2, even_w // 2, 2 * depth)
    zero_block = jnp.zeros((depth, depth), kernel.dtype)
    near = jnp.zeros((out_rows * (even_w // 2), depth), jnp.float32)
    far = jnp.zeros((out_rows * (even_w // 2), depth), jnp.float32)
    for row_tap in range(3):
        rows = pairs[row_tap // 2 : row_tap // 2 + out_rows, row_tap % 2]
        stacked = jnp.concatenate(
            [
                jnp.concatenate([kernel[row_tap, 0], kernel[row_tap, 2]], axis=1),
                jnp.concatenate([kernel[row_tap, 1], zero_block], axis=1),
            ],
            axis=0,
        )
        both = jnp.dot(rows.reshape(-1, 2 * depth), stacked, preferred_element_type=jnp.float32)
        near = near + both[:, :depth]
        far = far + both[:, depth:]
    near = near.reshape(out_rows, even_w // 2, depth)
    far = far.reshape(out_rows, even_w // 2, depth)
    return near[:, :out_cols] + far[:, 1 : out_cols + 1]


def encode_tile(grid, north, west, north_west, conv1_weight, conv2_weight):
    top = jnp.concatenate([north_west, north], axis=1)
    top = jnp.where(lax.axis_index("lat") == 0, jnp.zeros((), top.dtype), top)
    body_rows = jnp.concatenate([west, grid], axis=1)
    extended = jnp.concatenate([top, body_rows], axis=0)
    hidden = jax.nn.gelu(strided_valid(extended, conv1_weight)).astype(jnp.bfloat16)
    return strided_valid(hidden, conv2_weight).astype(jnp.bfloat16)


def body(
    radiances,
    project_weight,
    tile_ids,
    slot_offsets,
    tile_counts,
    setconv_weights,
    conv1_weight,
    conv2_weight,
):
    lat_size = lax.axis_size("lat")
    lon_size = lax.axis_size("lon")
    peer_count = lat_size * lon_size
    obs_count = radiances.shape[0]
    capacity = 7 * (obs_count // peer_count) // 2
    chunk_rows = ((capacity + 1 + 15) // 16) * 16
    slot_count = setconv_weights.shape[2]
    channel_count = project_weight.shape[1]
    digit = 64
    targets = jnp.arange(peer_count, dtype=jnp.int32)
    row_index = jnp.arange(obs_count, dtype=jnp.int32)
    matches = tile_ids[:, None] == targets[None, :]
    run_counts = jnp.sum(matches.astype(jnp.int32), axis=0)
    run_starts = jnp.min(jnp.where(matches, row_index[:, None], obs_count), axis=0)
    within = jnp.arange(chunk_rows, dtype=jnp.int32)
    source_rows = (run_starts[:, None] + within[None, :]).reshape(-1)
    valid_slot = (
        (within[None, :] < run_counts[:, None]) & (within[None, :] < capacity)
    ).reshape(-1)
    selector = (
        (source_rows[:, None] == row_index[None, :]) & valid_slot[:, None]
    ).astype(jnp.bfloat16)
    payload = jnp.dot(radiances, project_weight, preferred_element_type=jnp.float32).astype(
        jnp.bfloat16
    )
    key = slot_offsets + 1
    period = obs_count + 2 * capacity
    key_ext = jnp.concatenate([key, jnp.zeros((period - obs_count,), jnp.int32)])
    tiled_keys = jnp.tile(key_ext, capacity + 1)[: capacity * (period + 1)]
    hankel = tiled_keys.reshape(capacity, period + 1)[:, :obs_count].T
    windows = jnp.concatenate(
        [
            hankel // digit,
            hankel % digit,
            jnp.zeros((obs_count, channel_count - 2 * capacity), jnp.int32),
        ],
        axis=1,
    ).astype(jnp.bfloat16)
    run_head = (run_starts[:, None] == row_index[None, :]).astype(jnp.bfloat16)
    digit_row = jnp.dot(run_head, windows, preferred_element_type=jnp.float32)
    column = jnp.arange(channel_count, dtype=jnp.int32)
    digit_live = (column[None, :] % capacity < run_counts[:, None]) & (
        column[None, :] < 2 * capacity
    )
    digit_row = jnp.where(digit_live, digit_row, 0.0).astype(jnp.bfloat16)
    chunk_of = jnp.repeat(targets, chunk_rows)
    row_of = jnp.tile(within, peer_count)
    digit_pick = (row_of[:, None] == capacity) & (chunk_of[:, None] == targets[None, :])
    selector_all = jnp.concatenate([selector, digit_pick.astype(jnp.bfloat16)], axis=1)
    sources = jnp.concatenate([payload, digit_row], axis=0)
    outgoing = jnp.dot(selector_all, sources, preferred_element_type=jnp.float32).astype(
        jnp.bfloat16
    )
    outgoing = outgoing.reshape(peer_count, chunk_rows, channel_count)
    arrived = lax.all_to_all(outgoing, ("lat", "lon"), split_axis=0, concat_axis=0, tiled=True)
    arrived_rows = arrived[:, :capacity].reshape(-1, channel_count)
    arrived_digits = arrived[:, capacity].astype(jnp.int32)
    arrived_key = arrived_digits[:, :capacity] * digit + arrived_digits[:, capacity : 2 * capacity]
    arrived_offsets = arrived_key.reshape(-1) - 1
    slot_table = (
        jnp.arange(slot_count, dtype=jnp.int32)[:, None] == arrived_offsets[None, :]
    ).astype(jnp.bfloat16)
    obs_block = jnp.dot(slot_table, arrived_rows, preferred_element_type=jnp.float32).astype(
        jnp.bfloat16
    )
    tile_rows, tile_cols = (setconv_weights.shape[0], setconv_weights.shape[1])
    weights_flat = setconv_weights.reshape(-1, slot_count)
    live_mask = jnp.arange(slot_count, dtype=jnp.int32) < tile_counts.reshape(-1)[0]
    obs_masked = jnp.where(live_mask[:, None], obs_block, jnp.zeros((), jnp.bfloat16))
    masked = jnp.where(live_mask[None, :], weights_flat, jnp.zeros((), jnp.bfloat16))
    density = jnp.sum(masked, axis=1, dtype=jnp.float32)
    root = jnp.sqrt(density).reshape(tile_rows, tile_cols, 1)
    weights_cells = setconv_weights

    def cells(weights, roots):
        numer = jnp.dot(weights, obs_masked, preferred_element_type=jnp.float32)
        return (numer / roots).astype(jnp.bfloat16)

    rim = 3
    rim_weights = jnp.concatenate(
        [
            weights_cells[-rim:].reshape(-1, slot_count),
            weights_cells[:, -rim:].reshape(-1, slot_count),
        ],
        axis=0,
    )
    rim_roots = jnp.concatenate([root[-rim:].reshape(-1, 1), root[:, -rim:].reshape(-1, 1)], axis=0)
    rim_cells = cells(rim_weights, rim_roots)
    north_rows = rim_cells[: rim * tile_cols].reshape(rim, tile_cols, channel_count)
    west_cols = rim_cells[rim * tile_cols :].reshape(tile_rows, rim, channel_count)
    north = cyclic(north_rows, ("lat",), (1,))
    west = cyclic(west_cols, ("lon",), (1,))
    north_west = cyclic(north_rows[:, -rim:], ("lat", "lon"), (1, 1))
    grid = cells(weights_flat, root.reshape(-1, 1)).reshape(tile_rows, tile_cols, channel_count)
    return encode_tile(grid, north, west, north_west, conv1_weight, conv2_weight)


def solution(mesh):
    in_specs = (
        P(("lat", "lon"), None),
        P(),
        P(("lat", "lon")),
        P(("lat", "lon")),
        P("lat", "lon"),
        P("lat", "lon", None),
        P(),
        P(),
    )
    out_specs = P("lat", "lon", None)
    return jax.shard_map(body, mesh=mesh, in_specs=in_specs, out_specs=out_specs, check_vma=False)
```

```python
import jax
import jax.numpy as jnp
from jax import lax
from jax.sharding import PartitionSpec as P


def cyclic(value, axes, shifts):
    sizes = [lax.axis_size(a) for a in axes]
    pairs = []
    for l in range(sizes[0]):
        for n in range(sizes[-1] if len(axes) > 1 else 1):
            if len(axes) == 1:
                pairs.append((l, (l + shifts[0]) % sizes[0]))
            else:
                src = l * sizes[1] + n
                dst = ((l + shifts[0]) % sizes[0]) * sizes[1] + (n + shifts[1]) % sizes[1]
                pairs.append((src, dst))
    return lax.ppermute(value, axes if len(axes) > 1 else axes[0], pairs)


def strided_valid(field, kernel):
    height, breadth, depth = field.shape
    out_rows, out_cols = ((height - 3) // 2 + 1, (breadth - 3) // 2 + 1)
    even_h, even_w = (height + height % 2, breadth + breadth % 2)
    padded = jnp.pad(field, ((0, even_h - height), (0, even_w - breadth), (0, 0)))
    pairs = padded.reshape(even_h // 2, 2, even_w // 2, 2 * depth)
    zero_block = jnp.zeros((depth, depth), kernel.dtype)
    near = jnp.zeros((out_rows * (even_w // 2), depth), jnp.float32)
    far = jnp.zeros((out_rows * (even_w // 2), depth), jnp.float32)
    for row_tap in range(3):
        rows = pairs[row_tap // 2 : row_tap // 2 + out_rows, row_tap % 2]
        stacked = jnp.concatenate(
            [
                jnp.concatenate([kernel[row_tap, 0], kernel[row_tap, 2]], axis=1),
                jnp.concatenate([kernel[row_tap, 1], zero_block], axis=1),
            ],
            axis=0,
        )
        both = jnp.dot(rows.reshape(-1, 2 * depth), stacked, preferred_element_type=jnp.float32)
        near = near + both[:, :depth]
        far = far + both[:, depth:]
    near = near.reshape(out_rows, even_w // 2, depth)
    far = far.reshape(out_rows, even_w // 2, depth)
    return near[:, :out_cols] + far[:, 1 : out_cols + 1]


def encode_tile(grid, north, west, north_west, conv1_weight, conv2_weight):
    top = jnp.concatenate([north_west, north], axis=1)
    top = jnp.where(lax.axis_index("lat") == 0, jnp.zeros((), top.dtype), top)
    body_rows = jnp.concatenate([jnp.swapaxes(west, 0, 1), grid], axis=1)
    extended = jnp.concatenate([top, body_rows], axis=0)
    hidden = jax.nn.gelu(strided_valid(extended, conv1_weight)).astype(jnp.bfloat16)
    return strided_valid(hidden, conv2_weight).astype(jnp.bfloat16)


def body(
    radiances,
    project_weight,
    tile_ids,
    slot_offsets,
    tile_counts,
    setconv_weights,
    conv1_weight,
    conv2_weight,
):
    lat_size = lax.axis_size("lat")
    lon_size = lax.axis_size("lon")
    peer_count = lat_size * lon_size
    obs_count = radiances.shape[0]
    capacity = 7 * (obs_count // peer_count) // 2
    chunk_rows = ((capacity + 1 + 15) // 16) * 16
    slot_count = setconv_weights.shape[2]
    channel_count = project_weight.shape[1]
    digit = 64
    targets = jnp.arange(peer_count, dtype=jnp.int32)
    row_index = jnp.arange(obs_count, dtype=jnp.int32)
    matches = tile_ids[:, None] == targets[None, :]
    run_counts = jnp.sum(matches.astype(jnp.int32), axis=0)
    run_starts = jnp.min(jnp.where(matches, row_index[:, None], obs_count), axis=0)
    within = jnp.arange(chunk_rows, dtype=jnp.int32)
    source_rows = (run_starts[:, None] + within[None, :]).reshape(-1)
    valid_slot = (
        (within[None, :] < run_counts[:, None]) & (within[None, :] < capacity)
    ).reshape(-1)
    selector = (
        (source_rows[:, None] == row_index[None, :]) & valid_slot[:, None]
    ).astype(jnp.bfloat16)
    payload = jnp.dot(radiances, project_weight, preferred_element_type=jnp.float32).astype(
        jnp.bfloat16
    )
    key = slot_offsets + 1
    period = obs_count + 2 * capacity
    key_ext = jnp.concatenate([key, jnp.zeros((period - obs_count,), jnp.int32)])
    tiled_keys = jnp.tile(key_ext, capacity + 1)[: capacity * (period + 1)]
    hankel = tiled_keys.reshape(capacity, period + 1)[:, :obs_count].T
    windows = jnp.concatenate(
        [
            hankel // digit,
            hankel % digit,
            jnp.zeros((obs_count, channel_count - 2 * capacity), jnp.int32),
        ],
        axis=1,
    ).astype(jnp.bfloat16)
    run_head = (run_starts[:, None] == row_index[None, :]).astype(jnp.bfloat16)
    digit_row = jnp.dot(run_head, windows, preferred_element_type=jnp.float32)
    column = jnp.arange(channel_count, dtype=jnp.int32)
    digit_live = (column[None, :] % capacity < run_counts[:, None]) & (
        column[None, :] < 2 * capacity
    )
    digit_row = jnp.where(digit_live, digit_row, 0.0).astype(jnp.bfloat16)
    chunk_of = jnp.repeat(targets, chunk_rows)
    row_of = jnp.tile(within, peer_count)
    digit_pick = (row_of[:, None] == capacity) & (chunk_of[:, None] == targets[None, :])
    selector_all = jnp.concatenate([selector, digit_pick.astype(jnp.bfloat16)], axis=1)
    sources = jnp.concatenate([payload, digit_row], axis=0)
    outgoing = jnp.dot(selector_all, sources, preferred_element_type=jnp.float32).astype(
        jnp.bfloat16
    )
    outgoing = outgoing.reshape(peer_count, chunk_rows, channel_count)
    arrived = lax.all_to_all(outgoing, ("lat", "lon"), split_axis=0, concat_axis=0, tiled=True)
    arrived_rows = arrived[:, :capacity].reshape(-1, channel_count)
    arrived_digits = arrived[:, capacity].astype(jnp.int32)
    arrived_key = arrived_digits[:, :capacity] * digit + arrived_digits[:, capacity : 2 * capacity]
    arrived_offsets = arrived_key.reshape(-1) - 1
    slot_table = (
        jnp.arange(slot_count, dtype=jnp.int32)[:, None] == arrived_offsets[None, :]
    ).astype(jnp.bfloat16)
    obs_block = jnp.dot(slot_table, arrived_rows, preferred_element_type=jnp.float32).astype(
        jnp.bfloat16
    )
    tile_rows, tile_cols = (setconv_weights.shape[0], setconv_weights.shape[1])
    weights_flat = setconv_weights.reshape(-1, slot_count)
    live_mask = jnp.arange(slot_count, dtype=jnp.int32) < tile_counts.reshape(-1)[0]
    obs_masked = jnp.where(live_mask[:, None], obs_block, jnp.zeros((), jnp.bfloat16))
    masked = jnp.where(live_mask[None, :], weights_flat, jnp.zeros((), jnp.bfloat16))
    density = jnp.sum(masked, axis=1, dtype=jnp.float32)
    root = jnp.sqrt(density).reshape(tile_rows, tile_cols, 1)
    weights_cells = setconv_weights

    def cells(weights, roots):
        numer = jnp.dot(weights, obs_masked, preferred_element_type=jnp.float32)
        return (numer / roots).astype(jnp.bfloat16)

    rim = 3
    rim_weights = jnp.concatenate(
        [
            weights_cells[-rim:].reshape(-1, slot_count),
            jnp.swapaxes(weights_cells[:, -rim:], 0, 1).reshape(-1, slot_count),
        ],
        axis=0,
    )
    rim_roots = jnp.concatenate(
        [root[-rim:].reshape(-1, 1), jnp.swapaxes(root[:, -rim:], 0, 1).reshape(-1, 1)], axis=0
    )
    rim_cells = cells(rim_weights, rim_roots)
    north_rows = rim_cells[: rim * tile_cols].reshape(rim, tile_cols, channel_count)
    west_cols = rim_cells[rim * tile_cols :].reshape(rim, tile_rows, channel_count)
    north = cyclic(north_rows, ("lat",), (1,))
    west = cyclic(west_cols, ("lon",), (1,))
    north_west = cyclic(north_rows[:, -rim:], ("lat", "lon"), (1, 1))
    grid = cells(weights_flat, root.reshape(-1, 1)).reshape(tile_rows, tile_cols, channel_count)
    return encode_tile(grid, north, west, north_west, conv1_weight, conv2_weight)


def solution(mesh):
    in_specs = (
        P(("lat", "lon"), None),
        P(),
        P(("lat", "lon")),
        P(("lat", "lon")),
        P("lat", "lon"),
        P("lat", "lon", None),
        P(),
        P(),
    )
    out_specs = P("lat", "lon", None)
    return jax.shard_map(body, mesh=mesh, in_specs=in_specs, out_specs=out_specs, check_vma=False)
```

```python
import jax
import jax.numpy as jnp
from jax import lax
from jax.sharding import PartitionSpec as P


def cyclic(value, axes, shifts):
    sizes = [lax.axis_size(a) for a in axes]
    pairs = []
    for l in range(sizes[0]):
        for n in range(sizes[-1] if len(axes) > 1 else 1):
            if len(axes) == 1:
                pairs.append((l, (l + shifts[0]) % sizes[0]))
            else:
                src = l * sizes[1] + n
                dst = ((l + shifts[0]) % sizes[0]) * sizes[1] + (n + shifts[1]) % sizes[1]
                pairs.append((src, dst))
    return lax.ppermute(value, axes if len(axes) > 1 else axes[0], pairs)


def strided_valid(field, kernel):
    height, breadth, depth = field.shape
    out_rows, out_cols = ((height - 3) // 2 + 1, (breadth - 3) // 2 + 1)
    even_h, even_w = (height + height % 2, breadth + breadth % 2)
    padded = jnp.pad(field, ((0, even_h - height), (0, even_w - breadth), (0, 0)))
    pairs = padded.reshape(even_h // 2, 2, even_w // 2, 2 * depth)
    zero_block = jnp.zeros((depth, depth), kernel.dtype)
    near = jnp.zeros((out_rows * (even_w // 2), depth), jnp.float32)
    far = jnp.zeros((out_rows * (even_w // 2), depth), jnp.float32)
    for row_tap in range(3):
        rows = pairs[row_tap // 2 : row_tap // 2 + out_rows, row_tap % 2]
        stacked = jnp.concatenate(
            [
                jnp.concatenate([kernel[row_tap, 0], kernel[row_tap, 2]], axis=1),
                jnp.concatenate([kernel[row_tap, 1], zero_block], axis=1),
            ],
            axis=0,
        )
        both = jnp.dot(rows.reshape(-1, 2 * depth), stacked, preferred_element_type=jnp.float32)
        near = near + both[:, :depth]
        far = far + both[:, depth:]
    near = near.reshape(out_rows, even_w // 2, depth)
    far = far.reshape(out_rows, even_w // 2, depth)
    return near[:, :out_cols] + far[:, 1 : out_cols + 1]


def encode_tile(grid, north, west, north_west, conv1_weight, conv2_weight):
    top = jnp.concatenate([north_west, north], axis=1)
    top = jnp.where(lax.axis_index("lat") == 0, jnp.zeros((), top.dtype), top)
    body_rows = jnp.concatenate([west, grid], axis=1)
    extended = jnp.concatenate([top, body_rows], axis=0)
    hidden = jax.nn.gelu(strided_valid(extended, conv1_weight)).astype(jnp.bfloat16)
    return strided_valid(hidden, conv2_weight).astype(jnp.bfloat16)


def body(
    radiances,
    project_weight,
    tile_ids,
    slot_offsets,
    tile_counts,
    setconv_weights,
    conv1_weight,
    conv2_weight,
):
    lat_size = lax.axis_size("lat")
    lon_size = lax.axis_size("lon")
    peer_count = lat_size * lon_size
    obs_count = radiances.shape[0]
    capacity = 7 * (obs_count // peer_count) // 2
    chunk_rows = ((capacity + 1 + 15) // 16) * 16
    slot_count = setconv_weights.shape[2]
    channel_count = project_weight.shape[1]
    digit = 64
    targets = jnp.arange(peer_count, dtype=jnp.int32)
    row_index = jnp.arange(obs_count, dtype=jnp.int32)
    matches = tile_ids[:, None] == targets[None, :]
    run_counts = jnp.sum(matches.astype(jnp.int32), axis=0)
    run_starts = jnp.min(jnp.where(matches, row_index[:, None], obs_count), axis=0)
    within = jnp.arange(chunk_rows, dtype=jnp.int32)
    source_rows = (run_starts[:, None] + within[None, :]).reshape(-1)
    valid_slot = (
        (within[None, :] < run_counts[:, None]) & (within[None, :] < capacity)
    ).reshape(-1)
    selector = (
        (source_rows[:, None] == row_index[None, :]) & valid_slot[:, None]
    ).astype(jnp.bfloat16)
    payload = jnp.dot(radiances, project_weight, preferred_element_type=jnp.float32).astype(
        jnp.bfloat16
    )
    key = slot_offsets + 1
    period = obs_count + 2 * capacity
    key_ext = jnp.concatenate([key, jnp.zeros((period - obs_count,), jnp.int32)])
    tiled_keys = jnp.tile(key_ext, capacity + 1)[: capacity * (period + 1)]
    hankel = tiled_keys.reshape(capacity, period + 1)[:, :obs_count].T
    windows = jnp.concatenate(
        [
            hankel // digit,
            hankel % digit,
            jnp.zeros((obs_count, channel_count - 2 * capacity), jnp.int32),
        ],
        axis=1,
    ).astype(jnp.bfloat16)
    run_head = (run_starts[:, None] == row_index[None, :]).astype(jnp.bfloat16)
    digit_row = jnp.dot(run_head, windows, preferred_element_type=jnp.float32)
    column = jnp.arange(channel_count, dtype=jnp.int32)
    digit_live = (column[None, :] % capacity < run_counts[:, None]) & (
        column[None, :] < 2 * capacity
    )
    digit_row = jnp.where(digit_live, digit_row, 0.0).astype(jnp.bfloat16)
    chunk_of = jnp.repeat(targets, chunk_rows)
    row_of = jnp.tile(within, peer_count)
    digit_pick = (row_of[:, None] == capacity) & (chunk_of[:, None] == targets[None, :])
    selector_all = jnp.concatenate([selector, digit_pick.astype(jnp.bfloat16)], axis=1)
    sources = jnp.concatenate([payload, digit_row], axis=0)
    outgoing = jnp.dot(selector_all, sources, preferred_element_type=jnp.float32).astype(
        jnp.bfloat16
    )
    outgoing = outgoing.reshape(peer_count, chunk_rows, channel_count)
    arrived = lax.all_to_all(outgoing, ("lat", "lon"), split_axis=0, concat_axis=0, tiled=True)
    arrived_rows = arrived.reshape(-1, channel_count)
    arrived_digits = arrived[:, capacity].astype(jnp.int32)
    arrived_key = arrived_digits[:, :capacity] * digit + arrived_digits[:, capacity : 2 * capacity]
    arrived_key = jnp.concatenate(
        [arrived_key, jnp.zeros((peer_count, chunk_rows - capacity), jnp.int32)], axis=1
    )
    arrived_offsets = arrived_key.reshape(-1) - 1
    slot_table = (
        jnp.arange(slot_count, dtype=jnp.int32)[:, None] == arrived_offsets[None, :]
    ).astype(jnp.bfloat16)
    obs_block = jnp.dot(slot_table, arrived_rows, preferred_element_type=jnp.float32).astype(
        jnp.bfloat16
    )
    tile_rows, tile_cols = (setconv_weights.shape[0], setconv_weights.shape[1])
    weights_flat = setconv_weights.reshape(-1, slot_count)
    live_mask = jnp.arange(slot_count, dtype=jnp.int32) < tile_counts.reshape(-1)[0]
    obs_masked = jnp.where(live_mask[:, None], obs_block, jnp.zeros((), jnp.bfloat16))
    masked = jnp.where(live_mask[None, :], weights_flat, jnp.zeros((), jnp.bfloat16))
    density = jnp.sum(masked, axis=1, dtype=jnp.float32)
    root = jnp.sqrt(density).reshape(tile_rows, tile_cols, 1)
    weights_cells = setconv_weights

    def cells(weights, roots):
        numer = jnp.dot(weights, obs_masked, preferred_element_type=jnp.float32)
        return (numer / roots).astype(jnp.bfloat16)

    rim = 3
    rim_weights = jnp.concatenate(
        [
            weights_cells[-rim:].reshape(-1, slot_count),
            weights_cells[:, -rim:].reshape(-1, slot_count),
        ],
        axis=0,
    )
    rim_roots = jnp.concatenate([root[-rim:].reshape(-1, 1), root[:, -rim:].reshape(-1, 1)], axis=0)
    rim_cells = cells(rim_weights, rim_roots)
    north_rows = rim_cells[: rim * tile_cols].reshape(rim, tile_cols, channel_count)
    west_cols = rim_cells[rim * tile_cols :].reshape(tile_rows, rim, channel_count)
    north = cyclic(north_rows, ("lat",), (1,))
    west = cyclic(west_cols, ("lon",), (1,))
    north_west = cyclic(north_rows[:, -rim:], ("lat", "lon"), (1, 1))
    grid = cells(weights_flat, root.reshape(-1, 1)).reshape(tile_rows, tile_cols, channel_count)
    return encode_tile(grid, north, west, north_west, conv1_weight, conv2_weight)


def solution(mesh):
    in_specs = (
        P(("lat", "lon"), None),
        P(),
        P(("lat", "lon")),
        P(("lat", "lon")),
        P("lat", "lon"),
        P("lat", "lon", None),
        P(),
        P(),
    )
    out_specs = P("lat", "lon", None)
    return jax.shard_map(body, mesh=mesh, in_specs=in_specs, out_specs=out_specs, check_vma=False)
```

```python
import jax
import jax.numpy as jnp
from jax import lax
from jax.sharding import PartitionSpec as P


def cyclic(value, axes, shifts):
    sizes = [lax.axis_size(a) for a in axes]
    pairs = []
    for l in range(sizes[0]):
        for n in range(sizes[-1] if len(axes) > 1 else 1):
            if len(axes) == 1:
                pairs.append((l, (l + shifts[0]) % sizes[0]))
            else:
                src = l * sizes[1] + n
                dst = ((l + shifts[0]) % sizes[0]) * sizes[1] + (n + shifts[1]) % sizes[1]
                pairs.append((src, dst))
    return lax.ppermute(value, axes if len(axes) > 1 else axes[0], pairs)


def strided_valid(field, kernel):
    height, breadth, depth = field.shape
    out_rows, out_cols = ((height - 3) // 2 + 1, (breadth - 3) // 2 + 1)
    even_h, even_w = (height + height % 2, breadth + breadth % 2)
    padded = jnp.pad(field, ((0, even_h - height), (0, even_w - breadth), (0, 0)))
    pairs = padded.reshape(even_h // 2, 2, even_w // 2, 2 * depth)
    zero_block = jnp.zeros((depth, depth), kernel.dtype)
    near = jnp.zeros((out_rows, even_w // 2, depth), jnp.float32)
    far = jnp.zeros((out_rows, even_w // 2, depth), jnp.float32)
    for row_tap in range(3):
        rows = pairs[row_tap // 2 : row_tap // 2 + out_rows, row_tap % 2]
        stacked = jnp.concatenate(
            [
                jnp.concatenate([kernel[row_tap, 0], kernel[row_tap, 2]], axis=1),
                jnp.concatenate([kernel[row_tap, 1], zero_block], axis=1),
            ],
            axis=0,
        )
        both = jnp.einsum("ijc,cd->ijd", rows, stacked, preferred_element_type=jnp.float32)
        near = near + both[:, :, :depth]
        far = far + both[:, :, depth:]
    return near[:, :out_cols] + far[:, 1 : out_cols + 1]


def encode_tile(grid, north, west, north_west, conv1_weight, conv2_weight):
    top = jnp.concatenate([north_west, north], axis=1)
    top = jnp.where(lax.axis_index("lat") == 0, jnp.zeros((), top.dtype), top)
    body_rows = jnp.concatenate([west, grid], axis=1)
    extended = jnp.concatenate([top, body_rows], axis=0)
    hidden = jax.nn.gelu(strided_valid(extended, conv1_weight)).astype(jnp.bfloat16)
    return strided_valid(hidden, conv2_weight).astype(jnp.bfloat16)


def body(
    radiances,
    project_weight,
    tile_ids,
    slot_offsets,
    tile_counts,
    setconv_weights,
    conv1_weight,
    conv2_weight,
):
    lat_size = lax.axis_size("lat")
    lon_size = lax.axis_size("lon")
    peer_count = lat_size * lon_size
    obs_count = radiances.shape[0]
    capacity = 7 * (obs_count // peer_count) // 2
    chunk_rows = ((capacity + 1 + 15) // 16) * 16
    slot_count = setconv_weights.shape[2]
    channel_count = project_weight.shape[1]
    digit = 64
    targets = jnp.arange(peer_count, dtype=jnp.int32)
    row_index = jnp.arange(obs_count, dtype=jnp.int32)
    matches = tile_ids[:, None] == targets[None, :]
    run_counts = jnp.sum(matches.astype(jnp.int32), axis=0)
    run_starts = jnp.min(jnp.where(matches, row_index[:, None], obs_count), axis=0)
    within = jnp.arange(chunk_rows, dtype=jnp.int32)
    source_rows = (run_starts[:, None] + within[None, :]).reshape(-1)
    valid_slot = (
        (within[None, :] < run_counts[:, None]) & (within[None, :] < capacity)
    ).reshape(-1)
    selector = (
        (source_rows[:, None] == row_index[None, :]) & valid_slot[:, None]
    ).astype(jnp.bfloat16)
    payload = jnp.dot(radiances, project_weight, preferred_element_type=jnp.float32).astype(
        jnp.bfloat16
    )
    key = slot_offsets + 1
    period = obs_count + 2 * capacity
    key_ext = jnp.concatenate([key, jnp.zeros((period - obs_count,), jnp.int32)])
    tiled_keys = jnp.tile(key_ext, capacity + 1)[: capacity * (period + 1)]
    hankel = tiled_keys.reshape(capacity, period + 1)[:, :obs_count].T
    windows = jnp.concatenate(
        [
            hankel // digit,
            hankel % digit,
            jnp.zeros((obs_count, channel_count - 2 * capacity), jnp.int32),
        ],
        axis=1,
    ).astype(jnp.bfloat16)
    run_head = (run_starts[:, None] == row_index[None, :]).astype(jnp.bfloat16)
    digit_row = jnp.dot(run_head, windows, preferred_element_type=jnp.float32)
    column = jnp.arange(channel_count, dtype=jnp.int32)
    digit_live = (column[None, :] % capacity < run_counts[:, None]) & (
        column[None, :] < 2 * capacity
    )
    digit_row = jnp.where(digit_live, digit_row, 0.0).astype(jnp.bfloat16)
    chunk_of = jnp.repeat(targets, chunk_rows)
    row_of = jnp.tile(within, peer_count)
    digit_pick = (row_of[:, None] == capacity) & (chunk_of[:, None] == targets[None, :])
    selector_all = jnp.concatenate([selector, digit_pick.astype(jnp.bfloat16)], axis=1)
    sources = jnp.concatenate([payload, digit_row], axis=0)
    outgoing = jnp.dot(selector_all, sources, preferred_element_type=jnp.float32).astype(
        jnp.bfloat16
    )
    outgoing = outgoing.reshape(peer_count, chunk_rows, channel_count)
    arrived = lax.all_to_all(outgoing, ("lat", "lon"), split_axis=0, concat_axis=0, tiled=True)
    arrived_rows = arrived.reshape(-1, channel_count)
    arrived_digits = arrived[:, capacity].astype(jnp.int32)
    arrived_key = arrived_digits[:, :capacity] * digit + arrived_digits[:, capacity : 2 * capacity]
    arrived_key = jnp.concatenate(
        [arrived_key, jnp.zeros((peer_count, chunk_rows - capacity), jnp.int32)], axis=1
    )
    arrived_offsets = arrived_key.reshape(-1) - 1
    slot_table = (
        jnp.arange(slot_count, dtype=jnp.int32)[:, None] == arrived_offsets[None, :]
    ).astype(jnp.bfloat16)
    obs_block = jnp.dot(slot_table, arrived_rows, preferred_element_type=jnp.float32).astype(
        jnp.bfloat16
    )
    tile_rows, tile_cols = (setconv_weights.shape[0], setconv_weights.shape[1])
    weights_flat = setconv_weights.reshape(-1, slot_count)
    live_mask = jnp.arange(slot_count, dtype=jnp.int32) < tile_counts.reshape(-1)[0]
    obs_masked = jnp.where(live_mask[:, None], obs_block, jnp.zeros((), jnp.bfloat16))
    masked = jnp.where(live_mask[None, :], weights_flat, jnp.zeros((), jnp.bfloat16))
    density = jnp.sum(masked, axis=1, dtype=jnp.float32)
    root = jnp.sqrt(density).reshape(tile_rows, tile_cols, 1)
    weights_cells = setconv_weights

    def cells(weights, roots):
        numer = jnp.dot(weights, obs_masked, preferred_element_type=jnp.float32)
        return (numer / roots).astype(jnp.bfloat16)

    rim = 3
    rim_weights = jnp.concatenate(
        [
            weights_cells[-rim:].reshape(-1, slot_count),
            weights_cells[:, -rim:].reshape(-1, slot_count),
        ],
        axis=0,
    )
    rim_roots = jnp.concatenate([root[-rim:].reshape(-1, 1), root[:, -rim:].reshape(-1, 1)], axis=0)
    rim_cells = cells(rim_weights, rim_roots)
    north_rows = rim_cells[: rim * tile_cols].reshape(rim, tile_cols, channel_count)
    west_cols = rim_cells[rim * tile_cols :].reshape(tile_rows, rim, channel_count)
    north = cyclic(north_rows, ("lat",), (1,))
    west = cyclic(west_cols, ("lon",), (1,))
    north_west = cyclic(north_rows[:, -rim:], ("lat", "lon"), (1, 1))
    grid = cells(weights_flat, root.reshape(-1, 1)).reshape(tile_rows, tile_cols, channel_count)
    return encode_tile(grid, north, west, north_west, conv1_weight, conv2_weight)


def solution(mesh):
    in_specs = (
        P(("lat", "lon"), None),
        P(),
        P(("lat", "lon")),
        P(("lat", "lon")),
        P("lat", "lon"),
        P("lat", "lon", None),
        P(),
        P(),
    )
    out_specs = P("lat", "lon", None)
    return jax.shard_map(body, mesh=mesh, in_specs=in_specs, out_specs=out_specs, check_vma=False)
```
